32 devices in a mesh: ctx: 8 (over z, y), fsdp: 4 (over x, core).
Axes of the slice: x: 2, y: 2, z: 4, core: 2. Of those that a mesh axis runs over, the one named last changes fastest.
Arguments:
- tokens: bfloat16 [24, 1024, 896], P('fsdp', 'ctx'), may hold values from -6 to 6
- norm_one: bfloat16 [896], P('fsdp'), may hold values from 0.5 to 1.5
- query_weight: bfloat16 [896, 896], P('fsdp'), may hold values from -0.1875 to 0.1875
- query_bias: bfloat16 [896], P('fsdp'), may hold values from -3 to 3
- key_weight: bfloat16 [896, 128], P('fsdp'), may hold values from -0.1875 to 0.1875
- key_bias: bfloat16 [128], P('fsdp'), may hold values from -3 to 3
- value_weight: bfloat16 [896, 128], P('fsdp'), may hold values from -0.1875 to 0.1875
- value_bias: bfloat16 [128], P('fsdp'), may hold values from -3 to 3
- output_weight: bfloat16 [896, 896], P('fsdp'), may hold values from -0.75 to 0.75
- norm_two: bfloat16 [896], P('fsdp'), may hold values from 0.5 to 1.5
- gate_up: bfloat16 [2, 896, 4864], P(None, None, 'fsdp'), may hold values from -0.1875 to 0.1875
- down_weight: bfloat16 [4864, 896], P('fsdp'), may hold values from -0.078125 to 0.078125
- cotangent: bfloat16 [24, 1024, 896], P('fsdp', 'ctx'), may hold values from -6 to 6
Outputs:
- layer_out: bfloat16 [24, 1024, 896], P('fsdp', 'ctx')
- token_grad: float32 [24, 1024, 896], P('fsdp', 'ctx')
- norm_one_grad: float32 [896], P('fsdp')
- query_weight_grad: float32 [896, 896], P('fsdp')
- query_bias_grad: float32 [896], P('fsdp')
- key_weight_grad: float32 [896, 128], P('fsdp')
- key_bias_grad: float32 [128], P('fsdp')
- value_weight_grad: float32 [896, 128], P('fsdp')
- value_bias_grad: float32 [128], P('fsdp')
- output_weight_grad: float32 [896, 896], P('fsdp')
- norm_two_grad: float32 [896], P('fsdp')
- gate_up_grad: float32 [2, 896, 4864], P(None, None, 'fsdp')
- down_weight_grad: float32 [4864, 896], P('fsdp')
The draws below stay inside these ranges and needn't reach their ends.
All inputs are finite; a program needn't handle non-finite values.
Results may differ from the reference program's by a relative error of at most 0.03.
Values may be sent and summed in bfloat16 or wider, within the bound.
No kernel may reach another device: no remote copies, remote signals or barrier semaphores. Data moves between devices by JAX's collectives and lax.ppermute only.
A program may use at most 320 MiB of HBM per device.

```python
import jax
import jax.numpy as jnp
from jax import lax

D = 896
HEADS = 14
KV_HEADS = 2
HEAD_DIM = 64
FF = 4864
Q_WIDTH = 896
KV_WIDTH = 128
SEQ_LEN = 1024
SEQS = 24


def block_scale(stream_key, extent, shards, least, top_value):
    def one(position, blocks):
        draws = jax.random.uniform(jax.random.fold_in(jax.random.fold_in(stream_key, 6), position), (blocks,), jnp.float32, least / len(shards), top_value / len(shards))
        return jnp.repeat(jnp.exp(draws), extent[position] // blocks).reshape((-1,) + (1,) * (len(extent) - position - 1))

    level = one(*shards[0])
    for cut in shards[1:]:
        level = level * one(*cut)
    return level


def scatter_about(own_key, dims, deviation, bound, split=(), held_as=jnp.bfloat16):
    entries = jax.random.normal(own_key, dims, jnp.float32) * deviation
    if len(split) > 0:
        entries = block_scale(own_key, dims, split, -0.22, 0.18) * entries
    return jnp.clip(entries, min=-bound, max=bound).astype(held_as)


def setup_inputs(seed: int = 0) -> dict:
    streams_of = jax.random.split(jax.random.key(seed), 14)
    return {
        "tokens": scatter_about(streams_of[0], (SEQS, SEQ_LEN, D), 1.0, 6.0, ((0, 4), (1, 8))),
        "norm_one": jnp.clip(1.0 + 0.1 * jax.random.normal(streams_of[1], (D,), jnp.float32), 0.5, 1.5).astype(jnp.bfloat16),
        "query_weight": scatter_about(streams_of[2], (D, Q_WIDTH), D ** -0.5, 0.1875, ((0, 4),)),
        "query_bias": scatter_about(streams_of[3], (Q_WIDTH,), 0.5, 3.0, ((0, 4),)),
        "key_weight": scatter_about(streams_of[4], (D, KV_WIDTH), D ** -0.5, 0.1875, ((0, 4),)),
        "key_bias": scatter_about(streams_of[5], (KV_WIDTH,), 0.5, 3.0, ((0, 4),)),
        "value_weight": scatter_about(streams_of[6], (D, KV_WIDTH), D ** -0.5, 0.1875, ((0, 4),)),
        "value_bias": scatter_about(streams_of[7], (KV_WIDTH,), 0.5, 3.0, ((0, 4),)),
        "output_weight": scatter_about(streams_of[8], (Q_WIDTH, D), (Q_WIDTH // 16) ** -0.5, 0.75, ((0, 4),)),
        "norm_two": jnp.clip(1.0 + 0.1 * jax.random.normal(streams_of[9], (D,), jnp.float32), 0.5, 1.5).astype(jnp.bfloat16),
        "gate_up": scatter_about(streams_of[10], (2, D, FF), D ** -0.5, 0.1875, ((2, 4),)),
        "down_weight": scatter_about(streams_of[11], (FF, D), FF ** -0.5, 0.078125, ((0, 4),)),
        "cotangent": scatter_about(streams_of[12], (SEQS, SEQ_LEN, D), 1.0, 6.0, ((0, 4), (1, 8))),
    }


@jax.custom_vjp
def low(v):
    return lax.optimization_barrier(v.astype(jnp.bfloat16)).astype(jnp.float32)

@jax.custom_vjp
def low_back(v):
    return v

def low_keep(v):
    return (low(v), None)

def low_pass(kept, grad):
    return (grad,)

def back_keep(v):
    return (v, None)

def back_low(kept, grad):
    return (low(grad),)
low.defvjp(low_keep, low_pass)
low_back.defvjp(back_keep, back_low)
NORM_EPSILON = 1e-06
ROPE_BASE = 1000000.0
MASKED_SCORE = -1e+30
PRECISE = lax.Precision.HIGHEST

def rotary(positions):
    half_dim = HEAD_DIM // 2
    exponent = jnp.arange(half_dim, dtype=jnp.float32) * (2.0 / HEAD_DIM)
    frequency = ROPE_BASE ** (-exponent)
    angles = positions.astype(jnp.float32)[:, None] * frequency[None, :]
    angles = jnp.concatenate([angles, angles], axis=1)
    return (jnp.cos(angles), jnp.sin(angles))

def rotate(moving, cosine, sine_table):
    half_dim = moving.shape[-1] // 2
    turned = jnp.concatenate([-moving[..., half_dim:], moving[..., :half_dim]], axis=-1)
    return moving * cosine[:, None, :] + turned * sine_table[:, None, :]

def rms_norm(moving, gain):
    return moving * lax.rsqrt(lax.optimization_barrier(jnp.mean(moving * moving, axis=-1, keepdims=True)) + NORM_EPSILON) * gain

def attend_rows(query_block, first_row, key_rows, value_rows):
    raw_scores = jnp.einsum('qgjd,kgd->gjqk', query_block, key_rows, precision=PRECISE)
    scores = low_back(raw_scores) * HEAD_DIM ** (-0.5)
    query_pos = first_row + jnp.arange(query_block.shape[0], dtype=jnp.int32)
    key_pos = jnp.arange(key_rows.shape[0], dtype=jnp.int32)
    allowed = key_pos[None, :] <= query_pos[:, None]
    masked = jnp.where(allowed, scores, MASKED_SCORE)
    row_top = lax.optimization_barrier(jnp.max(masked, axis=-1, keepdims=True))
    weights = jnp.where(allowed, jnp.exp(masked - row_top), 0.0)
    row_total = lax.optimization_barrier(jnp.sum(weights, axis=-1, keepdims=True))
    mixed_out = jnp.einsum('gjqk,kgd->gjqd', low(weights), value_rows, precision=PRECISE) / row_total
    return jnp.transpose(mixed_out, (2, 0, 1, 3))

def layer_forward(tokens_f, norm_one, query_weight, query_bias, key_weight, key_bias, value_weight, value_bias, output_weight, norm_two, gate_up, down_weight):
    seq_length = tokens_f.shape[0]
    group_size = HEADS // KV_HEADS
    cosine, sine_table = rotary(jnp.arange(seq_length, dtype=jnp.int32))
    normed = low(rms_norm(tokens_f, norm_one))
    query_pre = low_back(jnp.dot(normed, query_weight, precision=PRECISE) + query_bias)
    key_pre = low_back(jnp.dot(normed, key_weight, precision=PRECISE) + key_bias)
    value_rows = low(low_back(jnp.dot(normed, value_weight, precision=PRECISE) + value_bias))
    query_rot = low(rotate(query_pre.reshape(seq_length, HEADS, HEAD_DIM), cosine, sine_table))
    key_rot = low(rotate(key_pre.reshape(seq_length, KV_HEADS, HEAD_DIM), cosine, sine_table))
    value_rows = value_rows.reshape(seq_length, KV_HEADS, HEAD_DIM)
    row_block = min(512, seq_length)
    block_count = seq_length // row_block
    query_blocks = query_rot.reshape(block_count, row_block, KV_HEADS, group_size, HEAD_DIM)
    block_starts = jnp.arange(block_count, dtype=jnp.int32) * row_block
    attend = jax.checkpoint(attend_rows)
    mixed_out = lax.map(lambda pair: attend(pair[0], pair[1], key_rot, value_rows), (query_blocks, block_starts))
    mixed_out = low(low_back(mixed_out.reshape(seq_length, Q_WIDTH)))
    branch = low_back(jnp.dot(mixed_out, output_weight, precision=PRECISE))
    hidden = tokens_f + branch
    normed_two = low(rms_norm(hidden, norm_two))
    gate_part = low_back(jnp.dot(normed_two, gate_up[0], precision=PRECISE))
    up_part = low_back(jnp.dot(normed_two, gate_up[1], precision=PRECISE))
    inner_act = low(jax.nn.silu(gate_part) * up_part)
    return hidden + jnp.dot(inner_act, down_weight, precision=PRECISE)

def reference(tokens, norm_one, query_weight, query_bias, key_weight, key_bias, value_weight, value_bias, output_weight, norm_two, gate_up, down_weight, cotangent):
    params = tuple((item.astype(jnp.float32) for item in (norm_one, query_weight, query_bias, key_weight, key_bias, value_weight, value_bias, output_weight, norm_two, gate_up, down_weight)))

    def one_sequence(carried, pair):
        seq_tokens, seq_cot = pair
        layer_val, pullback = jax.vjp(layer_forward, seq_tokens.astype(jnp.float32), params[0], params[1], params[2], params[3], params[4], params[5], params[6], params[7], params[8], params[9], params[10])
        grads = pullback(seq_cot.astype(jnp.float32))
        carried = tuple((older + newer for older, newer in zip(carried, grads[1:])))
        return (carried, (layer_val.astype(jnp.bfloat16), grads[0]))
    zeros_init = tuple((jnp.zeros(item.shape, jnp.float32) for item in params))
    totals, (layer_out, token_grad) = lax.scan(one_sequence, zeros_init, (tokens, cotangent))
    return (layer_out, token_grad, totals[0], totals[1], totals[2], totals[3], totals[4], totals[5], totals[6], totals[7], totals[8], totals[9], totals[10])
```

```python
import math

import jax
import jax.numpy as jnp
from jax import lax
from jax.sharding import PartitionSpec as P

HEADS = 14
KV_HEADS = 2
HEAD_DIM = 64


NORM_EPSILON = 1e-06
ROPE_BASE = 1000000.0
MASKED_SCORE = -1e30


def rotary(positions):
    half_dim = HEAD_DIM // 2
    exponent = jnp.arange(half_dim, dtype=jnp.float32) * (2.0 / HEAD_DIM)
    frequency = ROPE_BASE ** (-exponent)
    angles = positions.astype(jnp.float32)[:, None] * frequency[None, :]
    angles = jnp.concatenate([angles, angles], axis=1)
    return (jnp.cos(angles), jnp.sin(angles))


def rotate(moving, cosine, sine_table):
    half_dim = moving.shape[-1] // 2
    turned = jnp.concatenate([-moving[..., half_dim:], moving[..., :half_dim]], axis=-1)
    return moving * cosine[:, None, :] + turned * sine_table[:, None, :]


def rms_norm(moving, gain):
    return (
        moving * lax.rsqrt(jnp.mean(moving * moving, axis=-1, keepdims=True) + NORM_EPSILON) * gain
    )


def swish(gate_part, up_part):
    return jax.nn.silu(gate_part) * up_part


def mix_in(carried, key_rows, value_rows, query_heads, query_pos):
    seq_count, row_count, _ = key_rows.shape
    step_rows = math.gcd(row_count, 512)
    step_count = row_count // step_rows
    scale = HEAD_DIM ** (-0.5)

    def one_step(current, step_index):
        begin = step_index * step_rows

        def one_compute(present):
            row_top, row_total, summed = present
            key_part = lax.dynamic_slice_in_dim(
                key_rows, step_index * step_rows, step_rows, 1
            ).reshape(seq_count, step_rows, KV_HEADS, HEAD_DIM)
            value_part = lax.dynamic_slice_in_dim(
                value_rows, step_index * step_rows, step_rows, 1
            ).reshape(seq_count, step_rows, KV_HEADS, HEAD_DIM)
            scores = (
                jnp.einsum(
                    "sgjtd,srgd->sgjtr", query_heads, key_part, preferred_element_type=jnp.float32
                )
                * scale
            )
            allowed = (begin + jnp.arange(step_rows, dtype=jnp.int32))[None, :] <= query_pos[
                :, None
            ]
            masked = jnp.where(allowed, scores, MASKED_SCORE)
            new_top = jnp.maximum(row_top, jnp.max(masked, axis=-1))
            weights = jnp.where(allowed, jnp.exp(masked - new_top[..., None]), 0.0)
            rescale = jnp.exp(row_top - new_top)
            new_total = row_total * rescale + jnp.sum(weights, axis=-1)
            new_sum = summed * rescale[..., None] + jnp.einsum(
                "sgjtr,srgd->sgjtd",
                weights.astype(jnp.bfloat16),
                value_part,
                preferred_element_type=jnp.float32,
            )
            return (new_top, new_total, new_sum)

        return (
            lax.cond(begin <= query_pos[-1], one_compute, lambda kept_state: kept_state, current),
            None,
        )

    carried, _ = lax.scan(one_step, carried, jnp.arange(step_count, dtype=jnp.int32))
    return carried


def shards(
    tokens,
    norm_one,
    query_weight,
    query_bias,
    key_weight,
    key_bias,
    value_weight,
    value_bias,
    output_weight,
    norm_two,
    gate_up,
    down_weight,
    cotangent,
):
    seq_count, block_rows, model_width = tokens.shape
    group_size = HEADS // KV_HEADS
    kv_width = KV_HEADS * HEAD_DIM
    q_width = HEADS * HEAD_DIM
    scale = HEAD_DIM ** (-0.5)
    full_length = lax.axis_size("ctx") * block_rows
    query_pos = lax.axis_index("ctx") * block_rows + jnp.arange(block_rows, dtype=jnp.int32)
    cosine, sine_table = rotary(query_pos)
    (
        gain_one,
        query_full,
        qbias_full,
        key_full,
        kbias_full,
        value_full,
        vbias_full,
        output_full,
        gain_two,
    ) = (
        lax.all_gather(norm_one, "fsdp", axis=0, tiled=True),
        lax.all_gather(query_weight, "fsdp", axis=0, tiled=True),
        lax.all_gather(query_bias, "fsdp", axis=0, tiled=True),
        lax.all_gather(key_weight, "fsdp", axis=0, tiled=True),
        lax.all_gather(key_bias, "fsdp", axis=0, tiled=True),
        lax.all_gather(value_weight, "fsdp", axis=0, tiled=True),
        lax.all_gather(value_bias, "fsdp", axis=0, tiled=True),
        lax.all_gather(output_weight, "fsdp", axis=0, tiled=True),
        lax.all_gather(norm_two, "fsdp", axis=0, tiled=True),
    )
    tokens_f = tokens.astype(jnp.float32)
    normed, norm_pull = jax.vjp(rms_norm, tokens_f, gain_one.astype(jnp.float32))
    normed_low = normed.astype(jnp.bfloat16)
    query_pre = jnp.einsum(
        "std,de->ste", normed_low, query_full, preferred_element_type=jnp.float32
    ) + qbias_full.astype(jnp.float32)
    key_pre = jnp.einsum(
        "std,de->ste", normed_low, key_full, preferred_element_type=jnp.float32
    ) + kbias_full.astype(jnp.float32)
    value_pre = jnp.einsum(
        "std,de->ste", normed_low, value_full, preferred_element_type=jnp.float32
    ) + vbias_full.astype(jnp.float32)
    value_low = value_pre.astype(jnp.bfloat16)

    def turn(moving):
        return rotate(moving, cosine, sine_table)

    query_rot, query_turn_back = jax.vjp(
        turn, query_pre.reshape(seq_count, block_rows, HEADS, HEAD_DIM)
    )
    key_rot, key_turn_back = jax.vjp(
        turn, key_pre.reshape(seq_count, block_rows, KV_HEADS, HEAD_DIM)
    )
    query_heads = (
        query_rot.astype(jnp.bfloat16)
        .reshape(seq_count, block_rows, KV_HEADS, group_size, HEAD_DIM)
        .transpose(0, 2, 3, 1, 4)
    )
    key_low = key_rot.astype(jnp.bfloat16).reshape(seq_count, block_rows, kv_width)
    stat_shape = (seq_count, KV_HEADS, group_size, block_rows)
    init_state = (
        jnp.full(stat_shape, MASKED_SCORE, jnp.float32),
        jnp.zeros(stat_shape, jnp.float32),
        jnp.zeros(stat_shape + (HEAD_DIM,), jnp.float32),
    )
    row_top, row_total, summed = mix_in(
        init_state,
        lax.all_gather(key_low, "ctx", axis=1, tiled=True),
        lax.all_gather(value_low, "ctx", axis=1, tiled=True),
        query_heads,
        query_pos,
    )
    attention = summed / row_total[..., None]
    log_total = row_top + jnp.log(row_total)
    mixed_low = (
        attention.transpose(0, 3, 1, 2, 4)
        .reshape(seq_count, block_rows, q_width)
        .astype(jnp.bfloat16)
    )
    branch = jnp.einsum("ste,ed->std", mixed_low, output_full, preferred_element_type=jnp.float32)
    hidden = tokens_f + branch
    normed_two, norm_two_pull = jax.vjp(rms_norm, hidden, gain_two.astype(jnp.float32))
    normed_two_low = normed_two.astype(jnp.bfloat16)
    cot_f = cotangent.astype(jnp.float32)
    normed_two_all = lax.all_gather(normed_two_low, "fsdp", axis=0, tiled=True)
    cot_all = lax.all_gather(cotangent, "fsdp", axis=0, tiled=True)
    gate_part = jnp.einsum(
        "std,df->stf", normed_two_all, gate_up[0], preferred_element_type=jnp.float32
    )
    up_part = jnp.einsum(
        "std,df->stf", normed_two_all, gate_up[1], preferred_element_type=jnp.float32
    )
    inner_act, swish_pull = jax.vjp(swish, gate_part, up_part)
    inner_low = inner_act.astype(jnp.bfloat16)
    ffn_part = jnp.einsum("stf,fd->std", inner_low, down_weight, preferred_element_type=jnp.float32)
    ffn_term = lax.psum_scatter(
        ffn_part.astype(jnp.bfloat16), "fsdp", scatter_dimension=0, tiled=True
    ).astype(jnp.float32)
    grad_down = jnp.einsum("stf,std->fd", inner_low, cot_all, preferred_element_type=jnp.float32)
    grad_inner = jnp.einsum("std,fd->stf", cot_all, down_weight, preferred_element_type=jnp.float32)
    grad_gate, grad_up = swish_pull(grad_inner)
    grad_pair = jnp.stack([grad_gate, grad_up]).astype(jnp.bfloat16)
    grad_gate_up = jnp.einsum(
        "std,cstf->cdf", normed_two_all, grad_pair, preferred_element_type=jnp.float32
    )
    grad_normed_two_part = jnp.einsum(
        "cstf,cdf->std", grad_pair, gate_up, preferred_element_type=jnp.float32
    )
    grad_normed_two = lax.psum_scatter(
        grad_normed_two_part.astype(jnp.bfloat16), "fsdp", scatter_dimension=0, tiled=True
    ).astype(jnp.float32)
    layer_out = (hidden + ffn_term).astype(jnp.bfloat16)
    grad_hidden_norm, grad_gain_two = norm_two_pull(grad_normed_two)
    grad_hidden = cot_f + grad_hidden_norm
    grad_branch = grad_hidden.astype(jnp.bfloat16)
    grad_output = jnp.einsum(
        "ste,std->ed", mixed_low, grad_branch, preferred_element_type=jnp.float32
    )
    grad_mixed = jnp.einsum(
        "std,ed->ste", grad_branch, output_full, preferred_element_type=jnp.float32
    ).astype(jnp.bfloat16)
    grad_heads = grad_mixed.reshape(
        seq_count, block_rows, KV_HEADS, group_size, HEAD_DIM
    ).transpose(0, 2, 3, 1, 4)
    row_delta = jnp.sum(grad_heads.astype(jnp.float32) * attention, axis=-1)
    back_keys, back_values = (
        lax.all_gather(key_low, "ctx", axis=1, tiled=True),
        lax.all_gather(value_low, "ctx", axis=1, tiled=True),
    )
    step_rows = math.gcd(full_length, 512)

    def back_step(current, step_index):
        begin = step_index * step_rows

        def back_compute(present):
            grad_query, grad_kv = present
            key_part = lax.dynamic_slice_in_dim(back_keys, begin, step_rows, 1).reshape(
                seq_count, step_rows, KV_HEADS, HEAD_DIM
            )
            value_part = lax.dynamic_slice_in_dim(back_values, begin, step_rows, 1).reshape(
                seq_count, step_rows, KV_HEADS, HEAD_DIM
            )
            scores = (
                jnp.einsum(
                    "sgjtd,srgd->sgjtr", query_heads, key_part, preferred_element_type=jnp.float32
                )
                * scale
            )
            allowed = (begin + jnp.arange(step_rows, dtype=jnp.int32))[None, :] <= query_pos[
                :, None
            ]
            probs = jnp.where(allowed, jnp.exp(scores - log_total[..., None]), 0.0)
            grad_probs = jnp.einsum(
                "sgjtd,srgd->sgjtr", grad_heads, value_part, preferred_element_type=jnp.float32
            )
            grad_scores = (scale * probs * (grad_probs - row_delta[..., None])).astype(jnp.bfloat16)
            grad_query = grad_query + jnp.einsum(
                "sgjtr,srgd->sgjtd", grad_scores, key_part, preferred_element_type=jnp.float32
            )
            grad_key = jnp.einsum(
                "sgjtr,sgjtd->srgd", grad_scores, query_heads, preferred_element_type=jnp.float32
            )
            grad_value = jnp.einsum(
                "sgjtr,sgjtd->srgd",
                probs.astype(jnp.bfloat16),
                grad_heads,
                preferred_element_type=jnp.float32,
            )
            joined = jnp.concatenate(
                [
                    grad_key.reshape(seq_count, step_rows, kv_width),
                    grad_value.reshape(seq_count, step_rows, kv_width),
                ],
                axis=2,
            )
            return (grad_query, lax.dynamic_update_slice_in_dim(grad_kv, joined, begin, 1))

        return (
            lax.cond(begin <= query_pos[-1], back_compute, lambda kept_state: kept_state, current),
            None,
        )

    back_init = (
        jnp.zeros(stat_shape + (HEAD_DIM,), jnp.float32),
        jnp.zeros((seq_count, full_length, 2 * kv_width), jnp.float32),
    )
    (grad_query, grad_kv_all), _ = lax.scan(
        back_step, back_init, jnp.arange(full_length // step_rows, dtype=jnp.int32)
    )
    grad_kv = lax.psum_scatter(
        grad_kv_all.astype(jnp.bfloat16), "ctx", scatter_dimension=1, tiled=True
    ).astype(jnp.float32)
    grad_key_rot = grad_kv[..., :kv_width].reshape(seq_count, block_rows, KV_HEADS, HEAD_DIM)
    grad_key_low = (
        key_turn_back(grad_key_rot)[0].reshape(seq_count, block_rows, kv_width).astype(jnp.bfloat16)
    )
    grad_value_low = grad_kv[..., kv_width:].astype(jnp.bfloat16)
    grad_query_rot = grad_query.transpose(0, 3, 1, 2, 4).reshape(
        seq_count, block_rows, HEADS, HEAD_DIM
    )
    grad_query_low = (
        query_turn_back(grad_query_rot)[0]
        .reshape(seq_count, block_rows, q_width)
        .astype(jnp.bfloat16)
    )
    grad_qbias = jnp.sum(grad_query_low.astype(jnp.float32), axis=(0, 1))
    grad_kbias = jnp.sum(grad_key_low.astype(jnp.float32), axis=(0, 1))
    grad_vbias = jnp.sum(grad_value_low.astype(jnp.float32), axis=(0, 1))
    grad_qweight = jnp.einsum(
        "std,ste->de", normed_low, grad_query_low, preferred_element_type=jnp.float32
    )
    grad_kweight = jnp.einsum(
        "std,ste->de", normed_low, grad_key_low, preferred_element_type=jnp.float32
    )
    grad_vweight = jnp.einsum(
        "std,ste->de", normed_low, grad_value_low, preferred_element_type=jnp.float32
    )
    grad_normed = jnp.einsum(
        "ste,de->std", grad_query_low, query_full, preferred_element_type=jnp.float32
    )
    grad_normed = grad_normed + jnp.einsum(
        "ste,de->std", grad_key_low, key_full, preferred_element_type=jnp.float32
    )
    grad_normed = grad_normed + jnp.einsum(
        "ste,de->std", grad_value_low, value_full, preferred_element_type=jnp.float32
    )
    grad_tokens_norm, grad_gain_one = norm_pull(grad_normed)
    token_grad = grad_hidden + grad_tokens_norm
    (
        owned_gain_one,
        owned_qweight,
        owned_qbias,
        owned_kweight,
        owned_kbias,
        owned_vweight,
        owned_vbias,
        owned_output,
        owned_gain_two,
    ) = (
        lax.psum_scatter(
            grad_gain_one.astype(jnp.bfloat16), "fsdp", scatter_dimension=0, tiled=True
        ).astype(jnp.float32),
        lax.psum_scatter(
            grad_qweight.astype(jnp.bfloat16), "fsdp", scatter_dimension=0, tiled=True
        ).astype(jnp.float32),
        lax.psum_scatter(
            grad_qbias.astype(jnp.bfloat16), "fsdp", scatter_dimension=0, tiled=True
        ).astype(jnp.float32),
        lax.psum_scatter(
            grad_kweight.astype(jnp.bfloat16), "fsdp", scatter_dimension=0, tiled=True
        ).astype(jnp.float32),
        lax.psum_scatter(
            grad_kbias.astype(jnp.bfloat16), "fsdp", scatter_dimension=0, tiled=True
        ).astype(jnp.float32),
        lax.psum_scatter(
            grad_vweight.astype(jnp.bfloat16), "fsdp", scatter_dimension=0, tiled=True
        ).astype(jnp.float32),
        lax.psum_scatter(
            grad_vbias.astype(jnp.bfloat16), "fsdp", scatter_dimension=0, tiled=True
        ).astype(jnp.float32),
        lax.psum_scatter(
            grad_output.astype(jnp.bfloat16), "fsdp", scatter_dimension=0, tiled=True
        ).astype(jnp.float32),
        lax.psum_scatter(
            grad_gain_two.astype(jnp.bfloat16), "fsdp", scatter_dimension=0, tiled=True
        ).astype(jnp.float32),
    )
    (
        sum_gain_one,
        sum_qweight,
        sum_qbias,
        sum_kweight,
        sum_kbias,
        sum_vweight,
        sum_vbias,
        sum_output,
        sum_gain_two,
        sum_gate_up,
        sum_down,
    ) = (
        lax.psum(owned_gain_one.astype(jnp.bfloat16), "ctx").astype(jnp.float32),
        lax.psum(owned_qweight.astype(jnp.bfloat16), "ctx").astype(jnp.float32),
        lax.psum(owned_qbias.astype(jnp.bfloat16), "ctx").astype(jnp.float32),
        lax.psum(owned_kweight.astype(jnp.bfloat16), "ctx").astype(jnp.float32),
        lax.psum(owned_kbias.astype(jnp.bfloat16), "ctx").astype(jnp.float32),
        lax.psum(owned_vweight.astype(jnp.bfloat16), "ctx").astype(jnp.float32),
        lax.psum(owned_vbias.astype(jnp.bfloat16), "ctx").astype(jnp.float32),
        lax.psum(owned_output.astype(jnp.bfloat16), "ctx").astype(jnp.float32),
        lax.psum(owned_gain_two.astype(jnp.bfloat16), "ctx").astype(jnp.float32),
        lax.psum(grad_gate_up.astype(jnp.bfloat16), "ctx").astype(jnp.float32),
        lax.psum(grad_down.astype(jnp.bfloat16), "ctx").astype(jnp.float32),
    )
    return (
        layer_out,
        token_grad,
        sum_gain_one,
        sum_qweight,
        sum_qbias,
        sum_kweight,
        sum_kbias,
        sum_vweight,
        sum_vbias,
        sum_output,
        sum_gain_two,
        sum_gate_up,
        sum_down,
    )


def solution(mesh):
    placed = (
        P("fsdp", "ctx", None),
        P("fsdp"),
        P("fsdp", None),
        P("fsdp"),
        P("fsdp", None),
        P("fsdp"),
        P("fsdp", None),
        P("fsdp"),
        P("fsdp", None),
        P("fsdp"),
        P(None, None, "fsdp"),
        P("fsdp", None),
        P("fsdp", "ctx", None),
    )
    return jax.shard_map(
        shards,
        mesh=mesh,
        in_specs=placed,
        out_specs=(
            P("fsdp", "ctx", None),
            P("fsdp", "ctx", None),
            P("fsdp"),
            P("fsdp", None),
            P("fsdp"),
            P("fsdp", None),
            P("fsdp"),
            P("fsdp", None),
            P("fsdp"),
            P("fsdp", None),
            P("fsdp"),
            P(None, None, "fsdp"),
            P("fsdp", None),
        ),
        check_vma=False,
    )
```
